32 devices in a mesh: dp: 8 (over z, y), mp: 4 (over x, core).
Axes of the slice: x: 2, y: 2, z: 4, core: 2. Of those that a mesh axis runs over, the one named last changes fastest.
Arguments:
- tokens: bfloat16 [32, 512, 768], P('dp'), may hold values from -6 to 6
- prev_logits: bfloat16 [32, 12, 512, 512], P('dp', 'mp'), may hold values from -6 to 6
- segment_ids: int32 [32, 512], P('dp'), may hold values from -1 to 3, as said below
- w_qkv: bfloat16 [768, 3, 768], P(None, None, 'mp'), may hold values from -0.21875 to 0.21875
- bias_qv: bfloat16 [2, 768], P(None, 'mp'), may hold values from -3 to 3
- w_out: bfloat16 [768, 768], P('mp'), may hold values from -1.5 to 1.5
- b_out: bfloat16 [768], replicated, may hold values from -3 to 3
- gain_one: bfloat16 [768], replicated, may hold values from 0.25 to 1.75
- shift_one: bfloat16 [768], replicated, may hold values from -3 to 3
- w_in: bfloat16 [768, 3072], P(None, 'mp'), may hold values from -0.21875 to 0.21875
- b_in: bfloat16 [3072], P('mp'), may hold values from -3 to 3
- w_back: bfloat16 [3072, 768], P('mp'), may hold values from -0.109375 to 0.109375
- b_back: bfloat16 [768], replicated, may hold values from -3 to 3
- gain_two: bfloat16 [768], replicated, may hold values from 0.25 to 1.75
- shift_two: bfloat16 [768], replicated, may hold values from -3 to 3
- cotangent: bfloat16 [32, 512, 768], P('dp'), may hold values from -6 to 6
Outputs:
- output: bfloat16 [32, 512, 768], P('dp')
- raw_logits: bfloat16 [32, 12, 512, 512], P('dp', 'mp')
- grad_tokens: bfloat16 [32, 512, 768], P('dp')
- grad_prev: bfloat16 [32, 12, 512, 512], P('dp', 'mp')
- grad_w_qkv: float32 [768, 3, 768], P(None, None, 'mp')
- grad_bias_qv: float32 [2, 768], P(None, 'mp')
- grad_w_out: float32 [768, 768], P('mp')
- grad_b_out: float32 [768], replicated
- grad_gain_one: float32 [768], replicated
- grad_shift_one: float32 [768], replicated
- grad_w_in: float32 [768, 3072], P(None, 'mp')
- grad_b_in: float32 [3072], P('mp')
- grad_w_back: float32 [3072, 768], P('mp')
- grad_b_back: float32 [768], replicated
- grad_gain_two: float32 [768], replicated
- grad_shift_two: float32 [768], replicated
The draws below stay inside these ranges and needn't reach their ends.
Inputs may be any that keep to these rules, and one draw needn't show every extreme that they name: `segment_ids`: each row holds 4 documents numbered 0 to 3 in order, each a run of consecutive slots, followed by one or more padding slots marked -1 at the row's end.
All inputs are finite; a program needn't handle non-finite values.
Results may differ from the reference program's by a relative error of at most 0.014.
The reference program's roundings to bfloat16 on the way count: a program that leaves them out, or rounds other values in their place, can miss the bound.
Values sent between devices are 32-bit elements; how exact they have to be, the bound alone decides.
No kernel may reach another device: no remote copies, remote signals or barrier semaphores. Data moves between devices by JAX's collectives and lax.ppermute only.
A program may use at most 192 MiB of HBM per device.

```python
import jax
import jax.numpy as jnp
from jax import lax

D = 768
HEADS = 12
HEAD_DIM = 64
FF = 3072
SLOTS = 512
DOCS = 4
BATCH = 32


def draw_segment_ids(key, part):
    base = jax.random.fold_in(key, 7)
    first_key, second_key = jax.random.split(base)
    padding = jax.random.randint(first_key, (BATCH, 1), 1, SLOTS // 8 + 1)
    used = SLOTS - padding
    jitter = SLOTS // (8 * DOCS)
    offsets = jax.random.randint(second_key, (BATCH, DOCS - 1), -jitter, jitter + 1)
    starts = jnp.arange(1, DOCS, dtype=jnp.int32)[None, :] * used // DOCS + offsets
    places = jnp.arange(SLOTS, dtype=jnp.int32)
    numbers = jnp.sum((places[None, :, None] >= starts[:, None, :]).astype(jnp.int32), axis=-1)
    return jnp.where(places[None, :] < used, numbers, -1).astype(jnp.int32)


def level_of(stream_key, dims, cuts, smallest, top_value):
    factor_of = 1.0
    for position, shards_of in cuts:
        heights = jax.random.uniform(jax.random.fold_in(jax.random.fold_in(stream_key, 6), position), (shards_of,), jnp.float32, smallest / len(cuts), top_value / len(cuts))
        factor_of = factor_of * jnp.repeat(jnp.exp(heights), dims[position] // shards_of).reshape((-1,) + (1,) * (len(dims) - 1 - position))
    return factor_of


def normal_values(key, shape, deviation, reach, pieces=(), held_as=jnp.bfloat16):
    array = deviation * jax.random.normal(key, shape, jnp.float32)
    if pieces:
        array = array * level_of(key, shape, pieces, -0.22, 0.18)
    return jnp.clip(array, -reach, reach).astype(held_as)


def setup_inputs(seed: int = 0) -> dict:
    seeds = jax.random.split(jax.random.key(seed), 17)
    tokens = normal_values(seeds[0], (BATCH, SLOTS, D), 1.0, 6.0, ((0, 8),))
    prev_logits = normal_values(seeds[1], (BATCH, HEADS, SLOTS, SLOTS), 1.0, 6.0, ((0, 8), (1, 4)))
    segment_ids = draw_segment_ids(jax.random.fold_in(seeds[16], 71), 0)
    w_qkv = normal_values(seeds[3], (D, 3, HEADS * HEAD_DIM), D ** -0.5, 0.21875, ((2, 4),))
    bias_qv = normal_values(seeds[4], (2, HEADS * HEAD_DIM), 0.5, 3.0, ((1, 4),))
    w_out = normal_values(seeds[5], (HEADS * HEAD_DIM, D), (max(HEADS * HEAD_DIM // 48, 1)) ** -0.5, 1.5, ((0, 4),))
    b_out = normal_values(seeds[6], (D,), 0.5, 3.0)
    gain_one = jnp.clip(1.0 + 0.15 * jax.random.normal(seeds[7], (D,), jnp.float32), 0.25, 1.75).astype(jnp.bfloat16)
    shift_one = normal_values(seeds[8], (D,), 0.5, 3.0)
    w_in = normal_values(seeds[9], (D, FF), D ** -0.5, 0.21875, ((1, 4),))
    b_in = normal_values(seeds[10], (FF,), 0.5, 3.0, ((0, 4),))
    w_back = normal_values(seeds[11], (FF, D), FF ** -0.5, 0.109375, ((0, 4),))
    b_back = normal_values(seeds[12], (D,), 0.5, 3.0)
    gain_two = jnp.clip(1.0 + 0.15 * jax.random.normal(seeds[13], (D,), jnp.float32), 0.25, 1.75).astype(jnp.bfloat16)
    shift_two = normal_values(seeds[14], (D,), 0.5, 3.0)
    cotangent = normal_values(seeds[15], (BATCH, SLOTS, D), 1.0, 6.0, ((0, 8),))
    return dict(tokens=tokens, prev_logits=prev_logits, segment_ids=segment_ids, w_qkv=w_qkv, bias_qv=bias_qv, w_out=w_out, b_out=b_out, gain_one=gain_one, shift_one=shift_one, w_in=w_in, b_in=b_in, w_back=w_back, b_back=b_back, gain_two=gain_two, shift_two=shift_two, cotangent=cotangent)


@jax.custom_vjp
def low(v):
    return lax.optimization_barrier(v.astype(jnp.bfloat16)).astype(jnp.float32)

@jax.custom_vjp
def low_back(v):
    return v

def low_keep(v):
    return (low(v), None)

def low_pass(kept, grad):
    return (grad,)

def back_keep(v):
    return (v, None)

def back_low(kept, grad):
    return (low(grad),)
low.defvjp(low_keep, low_pass)
low_back.defvjp(back_keep, back_low)
highest = lax.Precision.HIGHEST

def normalize(hidden, gain, shift):
    average = lax.optimization_barrier(jnp.mean(hidden, axis=-1, keepdims=True))
    centred = hidden - average
    spread = lax.optimization_barrier(jnp.mean(centred * centred, axis=-1, keepdims=True))
    return centred * lax.rsqrt(spread + 1e-05) * gain + shift

def layer_row(tokens, previous, segment, params):
    w_qkv, bias_qv, w_out, b_out, gain_one, shift_one, w_in, b_in, w_back, b_back, gain_two, shift_two = params
    slots = tokens.shape[0]
    heads = previous.shape[0]
    projected = low_back(jnp.einsum('td,dch->tch', tokens, w_qkv, precision=highest))
    queries = low(projected[:, 0] + bias_qv[0]).reshape(slots, heads, -1)
    key_rows = low(projected[:, 1]).reshape(slots, heads, -1)
    values = low(projected[:, 2] + bias_qv[1]).reshape(slots, heads, -1)
    logits = low_back(jnp.einsum('qhe,khe->hqk', queries, key_rows, precision=highest)) * 0.125 + previous
    allowed = (segment[:, None] == segment[None, :]) & (segment[None, :] >= 0)
    scores = logits + jnp.where(allowed, 0.0, -10000.0)[None]
    weights = low(jax.nn.softmax(scores, axis=-1))
    context = low_back(jnp.einsum('hqk,khe->qhe', weights, values, precision=highest)).reshape(slots, -1)
    attended = low_back(jnp.dot(low(context), w_out, precision=highest))
    first = normalize(tokens + attended + b_out, gain_one, shift_one)
    inner = low_back(jnp.dot(low(first), w_in, precision=highest))
    active = jax.nn.gelu(inner + b_in, approximate=False)
    branch = low_back(jnp.dot(low(active), w_back, precision=highest))
    output = normalize(first + branch + b_back, gain_two, shift_two)
    return (output, logits)

def reference(tokens, prev_logits, segment_ids, w_qkv, bias_qv, w_out, b_out, gain_one, shift_one, w_in, b_in, w_back, b_back, gain_two, shift_two, cotangent):
    params = tuple((item.astype(jnp.float32) for item in (w_qkv, bias_qv, w_out, b_out, gain_one, shift_one, w_in, b_in, w_back, b_back, gain_two, shift_two)))
    tokens_f = tokens.astype(jnp.float32)
    previous_f = prev_logits.astype(jnp.float32)
    row_step = jax.checkpoint(layer_row)

    def forward(tokens_in, previous_in, weights_in):

        def step(carry, items):
            out_row, logit_row = row_step(items[0], items[1], items[2], weights_in)
            return (carry, (out_row, logit_row))
        unused, (outputs, logits) = lax.scan(step, jnp.zeros((), jnp.float32), (tokens_in, previous_in, segment_ids))
        return (outputs, logits)
    output, pullback, logits = jax.vjp(forward, tokens_f, previous_f, params, has_aux=True)
    grad_tok, grad_previous, grads = pullback(cotangent.astype(jnp.float32))
    g_qkv, g_bias, g_out, g_bout, g_gone, g_sone, g_in, g_bin, g_back, g_bback, g_gtwo, g_stwo = grads
    return (output.astype(jnp.bfloat16), logits.astype(jnp.bfloat16), grad_tok.astype(jnp.bfloat16), grad_previous.astype(jnp.bfloat16), g_qkv, g_bias, g_out, g_bout, g_gone, g_sone, g_in, g_bin, g_back, g_bback, g_gtwo, g_stwo)
```

```python
import functools

import jax
import jax.numpy as jnp
from jax import lax
from jax.sharding import PartitionSpec as P


def normalize(hidden, gain, shift):
    average = jnp.mean(hidden, axis=-1, keepdims=True)
    centred = hidden - average
    spread = jnp.mean(centred * centred, axis=-1, keepdims=True)
    return centred * lax.rsqrt(spread + 1e-05) * gain + shift


def gelu_exact(value):
    return jax.nn.gelu(value, approximate=False)


def mp_sum(value, parts):
    if parts != 4:
        return lax.psum(value, "mp")
    index = lax.axis_index("mp")
    core = index % 2
    half = value.shape[0] // 2
    mine = lax.dynamic_slice_in_dim(value, core * half, half)
    other = lax.dynamic_slice_in_dim(value, (1 - core) * half, half)
    chip_pairs = [(m, m ^ 1) for m in range(4)]
    cross_pairs = [(m, m ^ 2) for m in range(4)]
    mine = mine + lax.ppermute(other, "mp", chip_pairs)
    mine = mine + lax.ppermute(mine, "mp", cross_pairs)
    theirs = lax.ppermute(mine, "mp", chip_pairs)
    first = jnp.where(core == 0, mine, theirs)
    second = jnp.where(core == 0, theirs, mine)
    return jnp.concatenate([first, second], axis=0)


def dp_sum(arrays):
    flat = jnp.concatenate([item.reshape(-1) for item in arrays])
    summed = lax.psum(flat, "dp")
    out = []
    start = 0
    for item in arrays:
        out.append(summed[start : start + item.size].reshape(item.shape))
        start += item.size
    return out


def mask_for(segment):
    allowed = (segment[:, None] == segment[None, :]) & (segment[None, :] >= 0)
    return jnp.where(allowed, 0.0, -10000.0).astype(jnp.float32)


def row_scores(queries, key_rows, previous, segment):
    product = jnp.einsum("qhe,khe->hqk", queries, key_rows, preferred_element_type=jnp.float32)
    logits = product * 0.125 + previous.astype(jnp.float32)
    return (logits, logits + mask_for(segment)[None])


def attend_row(items):
    queries, key_rows, values, previous, segment = items
    logits, scores = row_scores(queries, key_rows, previous, segment)
    largest = jnp.max(scores, axis=-1, keepdims=True)
    total = jnp.sum(jnp.exp(scores - largest), axis=-1, keepdims=True)
    log_total = largest + jnp.log(total)
    weights = jnp.exp(scores - log_total).astype(jnp.bfloat16)
    context = jnp.einsum("hqk,khe->qhe", weights, values, preferred_element_type=jnp.float32)
    return (logits.astype(jnp.bfloat16), log_total, context.astype(jnp.bfloat16))


def attend_back_row(items):
    queries, key_rows, values, previous, segment, log_total, grad_context = items
    unused, scores = row_scores(queries, key_rows, previous, segment)
    weights = jnp.exp(scores - log_total)
    grad_weights = jnp.einsum(
        "qhe,khe->hqk", grad_context, values, preferred_element_type=jnp.float32
    )
    grad_values = jnp.einsum(
        "hqk,qhe->khe",
        weights.astype(jnp.bfloat16),
        grad_context,
        preferred_element_type=jnp.float32,
    )
    grad_scores = weights * (grad_weights - jnp.sum(weights * grad_weights, axis=-1, keepdims=True))
    scaled = (grad_scores * 0.125).astype(jnp.bfloat16)
    grad_queries = jnp.einsum("hqk,khe->qhe", scaled, key_rows, preferred_element_type=jnp.float32)
    grad_keys = jnp.einsum("hqk,qhe->khe", scaled, queries, preferred_element_type=jnp.float32)
    return (grad_scores.astype(jnp.bfloat16), grad_queries, grad_keys, grad_values)


def body(
    tokens,
    prev_logits,
    segment_ids,
    w_qkv,
    bias_qv,
    w_out,
    b_out,
    gain_one,
    shift_one,
    w_in,
    b_in,
    w_back,
    b_back,
    gain_two,
    shift_two,
    cotangent,
    parts=4,
):
    rows, slots, width = tokens.shape
    heads = prev_logits.shape[1]
    count = rows * slots
    flat = tokens.reshape(count, width)
    bias_f = bias_qv.astype(jnp.float32)
    projected = jnp.einsum("td,dch->tch", flat, w_qkv, preferred_element_type=jnp.float32)
    columns = projected.shape[2]
    head_dim = columns // heads

    def shaped(array):
        return array.reshape(rows, slots, heads, head_dim)

    queries = shaped((projected[:, 0] + bias_f[0]).astype(jnp.bfloat16))
    key_rows = shaped(projected[:, 1].astype(jnp.bfloat16))
    values = shaped((projected[:, 2] + bias_f[1]).astype(jnp.bfloat16))
    raw_logits, log_total, context = lax.map(
        attend_row, (queries, key_rows, values, prev_logits, segment_ids)
    )
    context = context.reshape(count, columns)
    attended = mp_sum(jnp.dot(context, w_out, preferred_element_type=jnp.float32), parts)
    hidden_one = flat.astype(jnp.float32) + attended + b_out.astype(jnp.float32)
    first, first_back = jax.vjp(
        normalize, hidden_one, gain_one.astype(jnp.float32), shift_one.astype(jnp.float32)
    )
    first_low = first.astype(jnp.bfloat16)
    inner = jnp.dot(first_low, w_in, preferred_element_type=jnp.float32) + b_in.astype(jnp.float32)
    active, gelu_back = jax.vjp(gelu_exact, inner)
    active_low = active.astype(jnp.bfloat16)
    branch = mp_sum(jnp.dot(active_low, w_back, preferred_element_type=jnp.float32), parts)
    hidden_two = first + branch + b_back.astype(jnp.float32)
    output, second_back = jax.vjp(
        normalize, hidden_two, gain_two.astype(jnp.float32), shift_two.astype(jnp.float32)
    )
    grad_two, grad_gain_two, grad_shift_two = second_back(
        cotangent.reshape(count, width).astype(jnp.float32)
    )
    grad_b_back = jnp.sum(grad_two, axis=0)
    grad_two_low = grad_two.astype(jnp.bfloat16)
    grad_w_back = jnp.einsum(
        "tf,td->fd", active_low, grad_two_low, preferred_element_type=jnp.float32
    )
    grad_active = jnp.einsum("td,fd->tf", grad_two_low, w_back, preferred_element_type=jnp.float32)
    (grad_inner,) = gelu_back(grad_active)
    grad_b_in = jnp.sum(grad_inner, axis=0)
    grad_inner_low = grad_inner.astype(jnp.bfloat16)
    grad_w_in = jnp.einsum(
        "td,tf->df", first_low, grad_inner_low, preferred_element_type=jnp.float32
    )
    ffn_group = dp_sum((grad_w_back, grad_b_back, grad_gain_two, grad_shift_two, grad_w_in, grad_b_in))
    grad_first = grad_two + mp_sum(
        jnp.einsum("tf,df->td", grad_inner_low, w_in, preferred_element_type=jnp.float32), parts
    )
    grad_one, grad_gain_one, grad_shift_one = first_back(grad_first)
    grad_b_out = jnp.sum(grad_one, axis=0)
    grad_one_low = grad_one.astype(jnp.bfloat16)
    grad_w_out = jnp.einsum("th,td->hd", context, grad_one_low, preferred_element_type=jnp.float32)
    out_group, ffn_group = lax.optimization_barrier(
        ((grad_w_out, grad_b_out, grad_gain_one, grad_shift_one), ffn_group)
    )
    out_group = dp_sum(out_group)
    grad_context = shaped(
        jnp.einsum("td,hd->th", grad_one_low, w_out, preferred_element_type=jnp.float32).astype(
            jnp.bfloat16
        )
    )
    grad_prev, grad_queries, grad_keys, grad_values = lax.map(
        attend_back_row,
        (queries, key_rows, values, prev_logits, segment_ids, log_total, grad_context),
    )
    grad_queries = grad_queries.reshape(count, columns)
    grad_keys = grad_keys.reshape(count, columns)
    grad_values = grad_values.reshape(count, columns)
    grad_bias_qv = jnp.stack([jnp.sum(grad_queries, axis=0), jnp.sum(grad_values, axis=0)], axis=0)
    grad_projected = jnp.stack([grad_queries, grad_keys, grad_values], axis=1).astype(jnp.bfloat16)
    grad_w_qkv = jnp.einsum("td,tch->dch", flat, grad_projected, preferred_element_type=jnp.float32)
    grad_input = grad_one + mp_sum(
        jnp.einsum("tch,dch->td", grad_projected, w_qkv, preferred_element_type=jnp.float32), parts
    )
    (qkv_group, out_group) = lax.optimization_barrier(((grad_w_qkv, grad_bias_qv), out_group))
    qkv_group = dp_sum(qkv_group)
    attn_group = (qkv_group[0], qkv_group[1]) + tuple(out_group)
    return (
        output.reshape(rows, slots, width).astype(jnp.bfloat16),
        raw_logits,
        grad_input.reshape(rows, slots, width).astype(jnp.bfloat16),
        grad_prev,
        attn_group[0],
        attn_group[1],
        attn_group[2],
        attn_group[3],
        attn_group[4],
        attn_group[5],
        ffn_group[4],
        ffn_group[5],
        ffn_group[0],
        ffn_group[1],
        ffn_group[2],
        ffn_group[3],
    )


def solution(mesh):
    in_specs = (
        P("dp", None, None),
        P("dp", "mp", None, None),
        P("dp", None),
        P(None, None, "mp"),
        P(None, "mp"),
        P("mp", None),
        P(),
        P(),
        P(),
        P(None, "mp"),
        P("mp"),
        P("mp", None),
        P(),
        P(),
        P(),
        P("dp", None, None),
    )
    out_specs = (
        P("dp", None, None),
        P("dp", "mp", None, None),
        P("dp", None, None),
        P("dp", "mp", None, None),
        P(None, None, "mp"),
        P(None, "mp"),
        P("mp", None),
        P(),
        P(),
        P(),
        P(None, "mp"),
        P("mp"),
        P("mp", None),
        P(),
        P(),
        P(),
    )
    step = functools.partial(body, parts=mesh.shape["mp"])
    return jax.shard_map(step, mesh=mesh, in_specs=in_specs, out_specs=out_specs, check_vma=False)
```

```python
import functools

import jax
import jax.numpy as jnp
from jax import lax
from jax.sharding import PartitionSpec as P


def normalize(hidden, gain, shift):
    average = jnp.mean(hidden, axis=-1, keepdims=True)
    centred = hidden - average
    spread = jnp.mean(centred * centred, axis=-1, keepdims=True)
    return centred * lax.rsqrt(spread + 1e-05) * gain + shift


def gelu_exact(value):
    return jax.nn.gelu(value, approximate=False)


def mp_sum(value, parts):
    if parts != 4:
        return lax.psum(value, "mp")
    index = lax.axis_index("mp")
    core = index % 2
    half = value.shape[0] // 2
    mine = lax.dynamic_slice_in_dim(value, core * half, half)
    other = lax.dynamic_slice_in_dim(value, (1 - core) * half, half)
    chip_pairs = [(m, m ^ 1) for m in range(4)]
    cross_pairs = [(m, m ^ 2) for m in range(4)]
    mine = mine + lax.ppermute(other, "mp", chip_pairs)
    mine = mine + lax.ppermute(mine, "mp", cross_pairs)
    theirs = lax.ppermute(mine, "mp", chip_pairs)
    first = jnp.where(core == 0, mine, theirs)
    second = jnp.where(core == 0, theirs, mine)
    return jnp.concatenate([first, second], axis=0)


def dp_sum(arrays):
    return list(lax.psum(tuple(arrays), "dp"))


def stacked(matrix, vectors):
    rows = [vector.reshape(-1, matrix.shape[-1]) for vector in vectors]
    return jnp.concatenate([matrix] + rows, axis=0)


def mask_for(segment):
    allowed = (segment[:, None] == segment[None, :]) & (segment[None, :] >= 0)
    return jnp.where(allowed, 0.0, -10000.0).astype(jnp.float32)


def row_scores(queries, key_rows, previous, segment):
    product = jnp.einsum("qhe,khe->hqk", queries, key_rows, preferred_element_type=jnp.float32)
    logits = product * 0.125 + previous.astype(jnp.float32)
    return (logits, logits + mask_for(segment)[None])


def attend_row(items):
    queries, key_rows, values, previous, segment = items
    logits, scores = row_scores(queries, key_rows, previous, segment)
    largest = jnp.max(scores, axis=-1, keepdims=True)
    total = jnp.sum(jnp.exp(scores - largest), axis=-1, keepdims=True)
    log_total = largest + jnp.log(total)
    weights = jnp.exp(scores - log_total).astype(jnp.bfloat16)
    context = jnp.einsum("hqk,khe->qhe", weights, values, preferred_element_type=jnp.float32)
    return (logits.astype(jnp.bfloat16), log_total, context.astype(jnp.bfloat16))


def attend_back_row(items):
    queries, key_rows, values, previous, segment, log_total, grad_context = items
    unused, scores = row_scores(queries, key_rows, previous, segment)
    weights = jnp.exp(scores - log_total)
    grad_weights = jnp.einsum(
        "qhe,khe->hqk", grad_context, values, preferred_element_type=jnp.float32
    )
    grad_values = jnp.einsum(
        "hqk,qhe->khe",
        weights.astype(jnp.bfloat16),
        grad_context,
        preferred_element_type=jnp.float32,
    )
    grad_scores = weights * (grad_weights - jnp.sum(weights * grad_weights, axis=-1, keepdims=True))
    scaled = (grad_scores * 0.125).astype(jnp.bfloat16)
    grad_queries = jnp.einsum("hqk,khe->qhe", scaled, key_rows, preferred_element_type=jnp.float32)
    grad_keys = jnp.einsum("hqk,qhe->khe", scaled, queries, preferred_element_type=jnp.float32)
    return (grad_scores.astype(jnp.bfloat16), grad_queries, grad_keys, grad_values)


def body(
    tokens,
    prev_logits,
    segment_ids,
    w_qkv,
    bias_qv,
    w_out,
    b_out,
    gain_one,
    shift_one,
    w_in,
    b_in,
    w_back,
    b_back,
    gain_two,
    shift_two,
    cotangent,
    parts=4,
):
    rows, slots, width = tokens.shape
    heads = prev_logits.shape[1]
    count = rows * slots
    flat = tokens.reshape(count, width)
    bias_f = bias_qv.astype(jnp.float32)
    projected = jnp.einsum("td,dch->tch", flat, w_qkv, preferred_element_type=jnp.float32)
    columns = projected.shape[2]
    head_dim = columns // heads

    def shaped(array):
        return array.reshape(rows, slots, heads, head_dim)

    queries = shaped((projected[:, 0] + bias_f[0]).astype(jnp.bfloat16))
    key_rows = shaped(projected[:, 1].astype(jnp.bfloat16))
    values = shaped((projected[:, 2] + bias_f[1]).astype(jnp.bfloat16))
    raw_logits, log_total, context = lax.map(
        attend_row, (queries, key_rows, values, prev_logits, segment_ids)
    )
    context = context.reshape(count, columns)
    attended = mp_sum(jnp.dot(context, w_out, preferred_element_type=jnp.float32), parts)
    hidden_one = flat.astype(jnp.float32) + attended + b_out.astype(jnp.float32)
    first, first_back = jax.vjp(
        normalize, hidden_one, gain_one.astype(jnp.float32), shift_one.astype(jnp.float32)
    )
    first_low = first.astype(jnp.bfloat16)
    inner = jnp.dot(first_low, w_in, preferred_element_type=jnp.float32) + b_in.astype(jnp.float32)
    active, gelu_back = jax.vjp(gelu_exact, inner)
    active_low = active.astype(jnp.bfloat16)
    branch = mp_sum(jnp.dot(active_low, w_back, preferred_element_type=jnp.float32), parts)
    hidden_two = first + branch + b_back.astype(jnp.float32)
    output, second_back = jax.vjp(
        normalize, hidden_two, gain_two.astype(jnp.float32), shift_two.astype(jnp.float32)
    )
    grad_two, grad_gain_two, grad_shift_two = second_back(
        cotangent.reshape(count, width).astype(jnp.float32)
    )
    grad_b_back = jnp.sum(grad_two, axis=0)
    grad_two_low = grad_two.astype(jnp.bfloat16)
    grad_w_back = jnp.einsum(
        "tf,td->fd", active_low, grad_two_low, preferred_element_type=jnp.float32
    )
    grad_active = jnp.einsum("td,fd->tf", grad_two_low, w_back, preferred_element_type=jnp.float32)
    (grad_inner,) = gelu_back(grad_active)
    grad_b_in = jnp.sum(grad_inner, axis=0)
    grad_inner_low = grad_inner.astype(jnp.bfloat16)
    grad_w_in = jnp.einsum(
        "td,tf->df", first_low, grad_inner_low, preferred_element_type=jnp.float32
    )
    grad_first = grad_two + mp_sum(
        jnp.einsum("tf,df->td", grad_inner_low, w_in, preferred_element_type=jnp.float32), parts
    )
    grad_one, grad_gain_one, grad_shift_one = first_back(grad_first)
    grad_b_out = jnp.sum(grad_one, axis=0)
    grad_one_low = grad_one.astype(jnp.bfloat16)
    grad_w_out = jnp.einsum("th,td->hd", context, grad_one_low, preferred_element_type=jnp.float32)
    width_rows = grad_w_back.shape[0]
    out_rows = grad_w_out.shape[0]
    back_stack = stacked(grad_w_back, (grad_b_back, grad_gain_two, grad_shift_two, grad_b_in))
    out_stack = stacked(grad_w_out, (grad_b_out, grad_gain_one, grad_shift_one))
    back_stack, out_stack, grad_w_in = dp_sum((back_stack, out_stack, grad_w_in))
    grad_w_back = back_stack[:width_rows]
    grad_b_back, grad_gain_two, grad_shift_two = (back_stack[width_rows + i] for i in range(3))
    grad_b_in = back_stack[width_rows + 3 :].reshape(-1)
    grad_w_out = out_stack[:out_rows]
    grad_b_out, grad_gain_one, grad_shift_one = (out_stack[out_rows + i] for i in range(3))
    ffn_group = (grad_w_back, grad_b_back, grad_gain_two, grad_shift_two, grad_w_in, grad_b_in)
    out_group = (grad_w_out, grad_b_out, grad_gain_one, grad_shift_one)
    grad_context = shaped(
        jnp.einsum("td,hd->th", grad_one_low, w_out, preferred_element_type=jnp.float32).astype(
            jnp.bfloat16
        )
    )
    grad_prev, grad_queries, grad_keys, grad_values = lax.map(
        attend_back_row,
        (queries, key_rows, values, prev_logits, segment_ids, log_total, grad_context),
    )
    grad_queries = grad_queries.reshape(count, columns)
    grad_keys = grad_keys.reshape(count, columns)
    grad_values = grad_values.reshape(count, columns)
    grad_bias_qv = jnp.stack([jnp.sum(grad_queries, axis=0), jnp.sum(grad_values, axis=0)], axis=0)
    grad_projected = jnp.stack([grad_queries, grad_keys, grad_values], axis=1).astype(jnp.bfloat16)
    grad_w_qkv = jnp.einsum("td,tch->dch", flat, grad_projected, preferred_element_type=jnp.float32)
    bias_rows = jnp.concatenate(
        [grad_bias_qv, jnp.zeros((1, grad_bias_qv.shape[1]), jnp.float32)], axis=0
    )
    qkv_stack = jnp.concatenate([grad_w_qkv, bias_rows[None]], axis=0)
    partial_input = jnp.einsum("tch,dch->td", grad_projected, w_qkv, preferred_element_type=jnp.float32)
    qkv_stack, out_group, ffn_group, partial_input = lax.optimization_barrier(
        (qkv_stack, out_group, ffn_group, partial_input)
    )
    (qkv_stack,) = dp_sum((qkv_stack,))
    grad_input = grad_one + mp_sum(partial_input, parts)
    attn_group = (qkv_stack[:-1], qkv_stack[-1, :2]) + tuple(out_group)
    return (
        output.reshape(rows, slots, width).astype(jnp.bfloat16),
        raw_logits,
        grad_input.reshape(rows, slots, width).astype(jnp.bfloat16),
        grad_prev,
        attn_group[0],
        attn_group[1],
        attn_group[2],
        attn_group[3],
        attn_group[4],
        attn_group[5],
        ffn_group[4],
        ffn_group[5],
        ffn_group[0],
        ffn_group[1],
        ffn_group[2],
        ffn_group[3],
    )


def solution(mesh):
    in_specs = (
        P("dp", None, None),
        P("dp", "mp", None, None),
        P("dp", None),
        P(None, None, "mp"),
        P(None, "mp"),
        P("mp", None),
        P(),
        P(),
        P(),
        P(None, "mp"),
        P("mp"),
        P("mp", None),
        P(),
        P(),
        P(),
        P("dp", None, None),
    )
    out_specs = (
        P("dp", None, None),
        P("dp", "mp", None, None),
        P("dp", None, None),
        P("dp", "mp", None, None),
        P(None, None, "mp"),
        P(None, "mp"),
        P("mp", None),
        P(),
        P(),
        P(),
        P(None, "mp"),
        P("mp"),
        P("mp", None),
        P(),
        P(),
        P(),
    )
    step = functools.partial(body, parts=mesh.shape["mp"])
    return jax.shard_map(step, mesh=mesh, in_specs=in_specs, out_specs=out_specs, check_vma=False)
```
